512 devices in a mesh: expert: 128 (over z, y, core), tensor: 4 (over x).
Axes of the slice: x: 4, y: 8, z: 8, core: 2. Of those that a mesh axis runs over, the one named last changes fastest.
Arguments:
- attn_partial: bfloat16 [4, 4096, 3584], P('tensor', 'expert'), may hold values from -4 to 4
- residual_in: bfloat16 [4096, 3584], P(('expert', 'tensor')), may hold values from -6 to 6
- norm_gain: bfloat16 [3584], replicated, may hold values from 0.25 to 1.75
- w_in: bfloat16 [128, 3584, 1024], P('expert', None, 'tensor'), may hold values from -0.09375 to 0.09375
- w_out: bfloat16 [128, 1024, 3584], P('expert', 'tensor'), may hold values from -0.375 to 0.375
- routes: int32 [4096, 8], P('expert'), may hold values from 0 to 127, all different within a row; in each aligned block of 32 rows (0 to 31, 32 to 63, ...) at most 4 rows name the same one
- gate_weights: float32 [4096, 8], P('expert'), may hold values from 0.05 to 0.5
Outputs:
- layer_out: bfloat16 [4096, 3584], P('expert')
The draws below stay inside these ranges and needn't reach their ends.
Inputs may be any that keep to these rules, and one draw needn't show every extreme that they name: `routes`: each row names 8 different experts. In each aligned block of 32 rows (the tokens of one index of expert) no expert is named by more than 4 rows, and in some block an expert is named by exactly 4 rows.
All inputs are finite; a program needn't handle non-finite values.
Results may differ from the reference program's by a relative error of at most 0.02.
Values may be sent and summed in bfloat16 or wider, within the bound.
No kernel may reach another device: no remote copies, remote signals or barrier semaphores. Data moves between devices by JAX's collectives and lax.ppermute only.
A program may use at most 64 MiB of HBM per device.

```python
import math
import jax
import jax.numpy as jnp
import numpy as np
from jax import lax

D = 3584
H = 1024
TOP = 8
QB = 128
TOKG = 32
TOKENS = 4096
EXPERTS = 128
CAP = 4
N_EXPERT = 128
N_TENSOR = 4


def level_of(own_key, shape, shards, least, top_value):
    gain = 1.0
    for dim, shards_of in shards:
        heights = jax.random.uniform(jax.random.fold_in(jax.random.fold_in(own_key, 6), dim), (shards_of,), jnp.float32, least / len(shards), top_value / len(shards))
        gain = gain * jnp.repeat(jnp.exp(heights), shape[dim] // shards_of).reshape((-1,) + (1,) * (len(shape) - 1 - dim))
    return gain


def shared_out(key, own, number, rows, count, top, most, skew):
    ranking = jax.random.permutation(key, count)
    crowded, usual = load_shares(count, rows * top, most, skew, True), load_shares(count, rows * top, most, skew, False)
    places = jnp.arange(count)

    def named(tallies, rotation):
        used = int((tallies > 0).sum())
        fixed = max(1, used // 4)
        shifted = fixed + (places - fixed + rotation * (used - fixed)) % max(1, count - fixed)
        return jnp.zeros((count,), jnp.int32).at[ranking[jnp.where(places < fixed, places, shifted)]].set(jnp.asarray(tallies, jnp.int32))

    tallies = jnp.where(number % 4 == 0, named(crowded, number // 4), named(usual, number - number // 4 - 1))
    mixed = jax.random.permutation(jax.random.fold_in(own, 3), count)
    donor, taker = mixed[0:count // 2 * 2:2], mixed[1:count // 2 * 2:2]
    margin = jnp.minimum(tallies[donor] - 1, most - tallies[taker]) // 2
    margin = jnp.where((donor == ranking[0]) | (taker == ranking[0]) | (tallies[taker] == 0), 0, jnp.maximum(margin, 0))
    shifted = jax.random.randint(jax.random.fold_in(own, 4), (count // 2,), 0, 1 << 20) % (margin + 1)
    tallies = tallies.at[donor].add(-shifted).at[taker].add(shifted)
    items = jnp.searchsorted(jnp.cumsum(tallies), jnp.arange(rows * top), side="right").astype(jnp.int32)
    table = items.reshape(top, rows).T
    table = table[jax.random.permutation(jax.random.fold_in(own, 1), rows)]
    rotation = jax.random.randint(jax.random.fold_in(own, 2), (rows, 1), 0, top)
    return jnp.take_along_axis(table, (jnp.arange(top)[None, :] + rotation) % top, axis=1)


def load_shares(count, total, most, skew, full):
    loads = [(1 << 20) // math.isqrt(grade ** skew) + 1 for grade in range(1, count + 1)]
    largest = most if full else min(most, max(-(-total // count), total * loads[0] // sum(loads)))
    least = 1 if total - largest >= count - 1 else 0
    given, surplus = [largest] + [least] * (count - 1), total - largest - least * (count - 1)
    while surplus > 0:
        free = [i for i in range(1, count) if given[i] < largest] or [i for i in range(1, count) if given[i] < most]
        pool, remaining = sum([loads[i] for i in free]), surplus
        for i in free:
            more = min(most - given[i], max(1, remaining * loads[i] // pool), surplus)
            given[i] = given[i] + more
            surplus = surplus - more
    return np.array(given)


def bell_draw(own_key, shape, spread, most, cuts=(), held_as=jnp.bfloat16):
    values = spread * jax.random.normal(own_key, shape, jnp.float32)
    if cuts:
        values = values * level_of(own_key, shape, cuts, -0.22, 0.18)
    return jnp.clip(values, -most, most).astype(held_as)


def setup_inputs(seed: int = 0) -> dict:
    seeds = jax.random.split(jax.random.key(seed), 8)
    attn_partial = bell_draw(seeds[0], (N_TENSOR, TOKENS, D), 0.5, 4.0, ((0, 4), (1, 128)))
    residual_in = bell_draw(seeds[1], (TOKENS, D), 1.0, 6.0, ((0, 512),))
    norm_gain = jnp.clip(1.0 + 0.15 * jax.random.normal(seeds[2], (D,), jnp.float32), 0.25, 1.75).astype(jnp.bfloat16)
    w_in = bell_draw(seeds[3], (EXPERTS, D, H), D ** -0.5, 0.09375, ((0, 128), (2, 4)))
    w_out = bell_draw(seeds[4], (EXPERTS, H, D), (H // 4) ** -0.5, 0.375, ((0, 128), (1, 4)))
    routes_keys = jax.random.split(jax.random.fold_in(seeds[5], 1), TOKENS // TOKG)
    routes_turns = jax.random.permutation(jax.random.fold_in(seeds[5], 3), TOKENS // TOKG)
    routes = jax.vmap(lambda own, number: shared_out(jax.random.fold_in(seeds[5], 2), own, number, TOKG, EXPERTS, TOP, CAP, 2))(routes_keys, routes_turns).reshape((TOKENS, TOP))
    gate_weights = jnp.clip(0.05 + 0.45 * jax.random.uniform(seeds[6], (TOKENS, TOP), jnp.float32) ** level_of(seeds[6], (TOKENS, TOP), ((0, 128),), -0.2, 0.2), 0.05, 0.5)
    return {"attn_partial": attn_partial, "residual_in": residual_in, "norm_gain": norm_gain, "w_in": w_in, "w_out": w_out, "routes": routes, "gate_weights": gate_weights}


def slot_tables(routes):
    pairs = routes.reshape(N_EXPERT, TOKG * TOP)
    onehot = (pairs[:, :, None] == jnp.arange(EXPERTS, dtype=jnp.int32)[None, None, :]).astype(jnp.int32)
    earlier = jnp.cumsum(onehot, axis=1) - onehot
    slot_index = lax.optimization_barrier(jnp.sum(earlier * onehot, axis=2)).astype(jnp.int32)
    target = (pairs * CAP + slot_index).astype(jnp.int32)
    group_ids = jnp.broadcast_to(jnp.arange(N_EXPERT, dtype=jnp.int32)[:, None], target.shape)
    pair_ids = jnp.arange(TOKENS * TOP, dtype=jnp.int32).reshape(N_EXPERT, TOKG * TOP)
    table = jnp.full((N_EXPERT, EXPERTS * CAP), -1, jnp.int32)
    return table.at[group_ids, target].set(pair_ids)

def reference(attn_partial, residual_in, norm_gain, w_in, w_out, routes, gate_weights):
    attention = lax.optimization_barrier(jnp.sum(attn_partial.astype(jnp.float32), axis=0))
    residual = (residual_in.astype(jnp.float32) + attention).astype(jnp.bfloat16)
    stream = residual.astype(jnp.float32)
    rms_value = jnp.sqrt(lax.optimization_barrier(jnp.mean(stream * stream, axis=1, keepdims=True)) + 1e-06)
    normed = stream / rms_value * norm_gain.astype(jnp.float32)
    blocks = normed.reshape(TOKENS, D // QB, QB)
    block_scale = (lax.optimization_barrier(jnp.max(jnp.abs(blocks), axis=2)) + 1e-06).astype(jnp.bfloat16)
    scale_wide = block_scale.astype(jnp.float32)[:, :, None]
    quantized = lax.optimization_barrier((blocks / scale_wide).astype(jnp.bfloat16))
    expert_input = (quantized.astype(jnp.float32) * scale_wide).reshape(TOKENS, D).astype(jnp.bfloat16)
    table = slot_tables(routes)
    gate_flat = gate_weights.reshape(-1).astype(jnp.float32)
    quarter = H // N_TENSOR

    def one_expert(index, total):
        slot_pairs = lax.dynamic_slice_in_dim(table, index * CAP, CAP, 1).reshape(-1)
        filled = slot_pairs >= 0
        safe_pairs = jnp.maximum(slot_pairs, 0)
        token_ids = (safe_pairs // TOP).astype(jnp.int32)
        row_block = jnp.where(filled[:, None], expert_input[token_ids], jnp.zeros((), jnp.bfloat16))
        weights_in = w_in[index]
        weights_out = w_out[index]
        hidden = jax.nn.silu(jnp.dot(row_block, weights_in, preferred_element_type=jnp.float32)).astype(jnp.bfloat16)
        summed = jnp.zeros((row_block.shape[0], D), jnp.float32)
        for lane in range(N_TENSOR):
            term = jnp.dot(hidden[:, lane * quarter:(lane + 1) * quarter], weights_out[lane * quarter:(lane + 1) * quarter], preferred_element_type=jnp.float32).astype(jnp.bfloat16)
            summed = summed + lax.optimization_barrier(term).astype(jnp.float32)
        expert_out = lax.optimization_barrier(summed.astype(jnp.bfloat16)).astype(jnp.float32)
        weight = jnp.where(filled, gate_flat[safe_pairs], jnp.zeros((), jnp.float32))
        return total.at[token_ids].add(expert_out * weight[:, None])
    mixture = lax.fori_loop(0, EXPERTS, one_expert, jnp.zeros((TOKENS, D), jnp.float32))
    return (stream + mixture).astype(jnp.bfloat16)
```

```python
import jax
import jax.numpy as jnp
from jax import lax
from jax.sharding import PartitionSpec as P

QB = 128


EPSILON = 1e-06


def capacity(group_tokens, top_count, expert_count):
    return min(group_tokens, max(4, 2 * group_tokens * top_count // expert_count))


def shards(attn_partial, residual_in, norm_gain, w_in, w_out, routes, gate_weights):
    group_tokens, top_count = routes.shape
    model_width = residual_in.shape[1]
    expert_count = lax.axis_size("expert")
    tensor_count = lax.axis_size("tensor")
    slot_count = capacity(group_tokens, top_count, expert_count)
    block_count = model_width // QB
    w_in_d = lax.all_to_all(w_in[0], "tensor", split_axis=0, concat_axis=1, tiled=True)
    w_out_d = lax.all_to_all(w_out[0], "tensor", split_axis=1, concat_axis=0, tiled=True)
    hidden_count = w_in_d.shape[1]
    hidden_quarter = hidden_count // tensor_count
    attention = lax.psum_scatter(
        attn_partial[0].astype(jnp.float32).astype(jnp.bfloat16),
        "tensor",
        scatter_dimension=0,
        tiled=True,
    ).astype(jnp.float32)
    residual = (residual_in.astype(jnp.float32) + attention).astype(jnp.bfloat16)
    stream = residual.astype(jnp.float32)
    rms_value = jnp.sqrt(jnp.mean(stream * stream, axis=1, keepdims=True) + EPSILON)
    normed = stream / rms_value * norm_gain.astype(jnp.float32)
    blocks = normed.reshape(-1, block_count, QB)
    block_scale = (jnp.max(jnp.abs(blocks), axis=2) + EPSILON).astype(jnp.bfloat16)
    scale_wide = block_scale.astype(jnp.float32)[:, :, None]
    quantized = (blocks / scale_wide).astype(jnp.bfloat16)
    expert_input = (
        (quantized.astype(jnp.float32) * scale_wide).reshape(-1, model_width).astype(jnp.bfloat16)
    )
    both = lax.all_to_all(
        jnp.stack([expert_input, residual]), "tensor", split_axis=2, concat_axis=1, tiled=True
    )
    group_input, group_resid = both[0], both[1]
    pair_expert = routes.reshape(-1)
    onehot = (pair_expert[:, None] == jnp.arange(expert_count, dtype=jnp.int32)[None, :]).astype(
        jnp.int32
    )
    earlier = jnp.cumsum(onehot, axis=0) - onehot
    slot_index = jnp.sum(earlier * onehot, axis=1)
    target = pair_expert * slot_count + slot_index
    pair_total = group_tokens * top_count
    slot_table = (
        jnp.full((expert_count * slot_count,), -1, jnp.int32)
        .at[target]
        .set(jnp.arange(pair_total, dtype=jnp.int32))
    )
    slot_table = slot_table.reshape(expert_count, slot_count)
    filled = slot_table >= 0
    token_ids = jnp.maximum(slot_table, 0) // top_count
    row_block = jnp.where(filled[:, :, None], group_input[token_ids], jnp.zeros((), jnp.bfloat16))
    recv_rows = lax.all_to_all(row_block, "expert", split_axis=0, concat_axis=0, tiled=True)
    sources = recv_rows.shape[0]
    quarter = recv_rows.shape[2]
    rows = recv_rows.reshape(sources * slot_count, quarter)
    pre_partial = jnp.dot(rows, w_in_d, preferred_element_type=jnp.float32)
    pre_value = lax.psum_scatter(pre_partial, "tensor", scatter_dimension=1, tiled=True)
    hidden_part = jax.nn.silu(pre_value).astype(jnp.bfloat16)
    hidden = lax.all_gather(hidden_part, "tensor", axis=1, tiled=True)
    summed = jnp.zeros((rows.shape[0], quarter), jnp.float32)
    for lane in range(tensor_count):
        lo = lane * hidden_quarter
        term = jnp.dot(
            hidden[:, lo : lo + hidden_quarter],
            w_out_d[lo : lo + hidden_quarter],
            preferred_element_type=jnp.float32,
        ).astype(jnp.bfloat16)
        summed = summed + term.astype(jnp.float32)
    expert_out = summed.astype(jnp.bfloat16).reshape(sources, slot_count, quarter)
    returned = lax.all_to_all(expert_out, "expert", split_axis=0, concat_axis=0, tiled=True)
    flat_back = returned.reshape(expert_count * slot_count, quarter)
    picked = flat_back[target].astype(jnp.float32) * gate_weights.reshape(-1)[:, None]
    mixture = jnp.sum(picked.reshape(group_tokens, top_count, quarter), axis=1)
    out_part = (group_resid.astype(jnp.float32) + mixture).astype(jnp.bfloat16)
    return lax.all_gather(out_part, "tensor", axis=1, tiled=True)


def solution(mesh):
    return jax.shard_map(
        shards,
        mesh=mesh,
        in_specs=(
            P("tensor", "expert", None),
            P(("expert", "tensor"), None),
            P(),
            P("expert", None, "tensor"),
            P("expert", "tensor", None),
            P("expert", None),
            P("expert", None),
        ),
        out_specs=P("expert", None),
        check_vma=False,
    )
```

```python
import jax
import jax.numpy as jnp
from jax import lax
from jax.sharding import PartitionSpec as P

QB = 128


EPSILON = 1e-06


def capacity(group_tokens, top_count, expert_count):
    return min(group_tokens, max(4, 2 * group_tokens * top_count // expert_count))


def layer(attn_partial, residual_in, norm_gain, w_in, w_out, routes, gate_weights):
    group_tokens, top_count = routes.shape
    model_width = residual_in.shape[1]
    expert_count = lax.axis_size("expert")
    tensor_count = lax.axis_size("tensor")
    slot_count = capacity(group_tokens, top_count, expert_count)
    block_count = model_width // QB
    w_stack = jnp.stack([w_in[0], w_out[0].T])
    hidden_quarter = w_stack.shape[2]
    width_quarter = model_width // tensor_count
    own = lax.axis_index("tensor")
    pieces = [lax.dynamic_slice_in_dim(w_stack, own * width_quarter, width_quarter, axis=1)]
    for shift in range(1, tensor_count):
        chunk = lax.dynamic_slice_in_dim(
            w_stack, ((own + shift) % tensor_count) * width_quarter, width_quarter, axis=1
        )
        ring = [(u, (u + shift) % tensor_count) for u in range(tensor_count)]
        pieces.append(lax.ppermute(chunk, "tensor", ring))
    by_shift = jnp.stack(pieces)
    w_blocks = by_shift[(own - jnp.arange(tensor_count)) % tensor_count]
    w_in_d = jnp.concatenate([w_blocks[j, 0] for j in range(tensor_count)], axis=1)
    head_terms = lax.all_to_all(
        attn_partial[0].reshape(tensor_count, -1, model_width), "tensor", split_axis=0, concat_axis=0
    )
    attention = jnp.sum(head_terms.astype(jnp.float32), axis=0)
    residual = (residual_in.astype(jnp.float32) + attention).astype(jnp.bfloat16)
    stream = residual.astype(jnp.float32)
    rms_value = jnp.sqrt(jnp.mean(stream * stream, axis=1, keepdims=True) + EPSILON)
    normed = stream / rms_value * norm_gain.astype(jnp.float32)
    blocks = normed.reshape(-1, block_count, QB)
    block_scale = (jnp.max(jnp.abs(blocks), axis=2) + EPSILON).astype(jnp.bfloat16)
    scale_wide = block_scale.astype(jnp.float32)[:, :, None]
    quantized = (blocks / scale_wide).astype(jnp.bfloat16)
    expert_input = (
        (quantized.astype(jnp.float32) * scale_wide).reshape(-1, model_width).astype(jnp.bfloat16)
    )
    both_rows = jnp.stack([expert_input, residual])
    both = lax.all_to_all(both_rows, "tensor", split_axis=2, concat_axis=1, tiled=True)
    group_input, group_resid = both[0], both[1]
    pair_expert = routes.reshape(-1)
    onehot = (pair_expert[:, None] == jnp.arange(expert_count, dtype=jnp.int32)[None, :]).astype(
        jnp.int32
    )
    earlier = jnp.cumsum(onehot, axis=0) - onehot
    slot_index = jnp.sum(earlier * onehot, axis=1)
    target = pair_expert * slot_count + slot_index
    pair_total = group_tokens * top_count
    slot_table = (
        jnp.full((expert_count * slot_count,), -1, jnp.int32)
        .at[target]
        .set(jnp.arange(pair_total, dtype=jnp.int32))
    )
    slot_table = slot_table.reshape(expert_count, slot_count)
    filled = slot_table >= 0
    token_ids = jnp.maximum(slot_table, 0) // top_count
    row_block = jnp.where(filled[:, :, None], group_input[token_ids], jnp.zeros((), jnp.bfloat16))
    recv_rows = lax.all_to_all(row_block, "expert", split_axis=0, concat_axis=0, tiled=True)
    sources = recv_rows.shape[0]
    quarter = recv_rows.shape[2]
    rows = recv_rows.reshape(sources * slot_count, quarter)
    pre_partial = jnp.dot(rows, w_in_d, preferred_element_type=jnp.float32)
    pre_value = lax.psum_scatter(
        pre_partial.astype(jnp.bfloat16), "tensor", scatter_dimension=1, tiled=True
    ).astype(jnp.float32)
    hidden_part = jax.nn.silu(pre_value).astype(jnp.bfloat16)
    hidden = lax.all_gather(hidden_part, "tensor", axis=1, tiled=True)
    summed = jnp.zeros((rows.shape[0], quarter), jnp.float32)
    for lane in range(tensor_count):
        lo = lane * hidden_quarter
        term = lax.dot_general(
            hidden[:, lo : lo + hidden_quarter],
            w_blocks[lane, 1],
            (((1,), (1,)), ((), ())),
            preferred_element_type=jnp.float32,
        ).astype(jnp.bfloat16)
        summed = summed + term.astype(jnp.float32)
    expert_out = summed.astype(jnp.bfloat16).reshape(sources, slot_count, quarter)
    returned = lax.all_to_all(expert_out, "expert", split_axis=0, concat_axis=0, tiled=True)
    flat_back = returned.reshape(expert_count * slot_count, quarter)
    picked = flat_back[target].astype(jnp.float32) * gate_weights.reshape(-1)[:, None]
    mixture = jnp.sum(picked.reshape(group_tokens, top_count, quarter), axis=1)
    out_part = (group_resid.astype(jnp.float32) + mixture).astype(jnp.bfloat16)
    return lax.all_gather(out_part, "tensor", axis=1, tiled=True)


def solution(mesh):
    return jax.shard_map(
        layer,
        mesh=mesh,
        in_specs=(
            P("tensor", "expert", None),
            P(("expert", "tensor"), None),
            P(),
            P("expert", None, "tensor"),
            P("expert", "tensor", None),
            P("expert", None),
            P("expert", None),
        ),
        out_specs=P("expert", None),
        check_vma=False,
    )
```

```python
import jax
import jax.numpy as jnp
from jax import lax
from jax.sharding import PartitionSpec as P

QB = 128


EPSILON = 1e-06


def capacity(group_tokens, top_count, expert_count):
    return min(group_tokens, max(4, 2 * group_tokens * top_count // expert_count))


def layer(attn_partial, residual_in, norm_gain, w_in, w_out, routes, gate_weights):
    group_tokens, top_count = routes.shape
    model_width = residual_in.shape[1]
    expert_count = lax.axis_size("expert")
    tensor_count = lax.axis_size("tensor")
    slot_count = capacity(group_tokens, top_count, expert_count)
    block_count = model_width // QB
    w_stack = jnp.stack([w_in[0], w_out[0].T])
    width_quarter = model_width // tensor_count
    own = lax.axis_index("tensor")
    pieces = [lax.dynamic_slice_in_dim(w_stack, own * width_quarter, width_quarter, axis=1)]
    for shift in range(1, tensor_count):
        chunk = lax.dynamic_slice_in_dim(
            w_stack, ((own + shift) % tensor_count) * width_quarter, width_quarter, axis=1
        )
        ring = [(u, (u + shift) % tensor_count) for u in range(tensor_count)]
        pieces.append(lax.ppermute(chunk, "tensor", ring))
    by_shift = jnp.stack(pieces)
    w_blocks = by_shift[(own - jnp.arange(tensor_count)) % tensor_count]

    head_terms = lax.all_to_all(
        attn_partial[0].reshape(tensor_count, -1, model_width), "tensor", split_axis=0, concat_axis=0
    )
    attention = jnp.sum(head_terms.astype(jnp.float32), axis=0)
    residual = (residual_in.astype(jnp.float32) + attention).astype(jnp.bfloat16)
    stream = residual.astype(jnp.float32)
    rms_value = jnp.sqrt(jnp.mean(stream * stream, axis=1, keepdims=True) + EPSILON)
    normed = stream / rms_value * norm_gain.astype(jnp.float32)
    blocks = normed.reshape(-1, block_count, QB)
    block_scale = (jnp.max(jnp.abs(blocks), axis=2) + EPSILON).astype(jnp.bfloat16)
    scale_wide = block_scale.astype(jnp.float32)[:, :, None]
    quantized = (blocks / scale_wide).astype(jnp.bfloat16)
    expert_input = (
        (quantized.astype(jnp.float32) * scale_wide).reshape(-1, model_width).astype(jnp.bfloat16)
    )
    both_rows = jnp.stack([expert_input, residual])
    both = lax.all_to_all(both_rows, "tensor", split_axis=2, concat_axis=1, tiled=True)
    group_input, group_resid = both[0], both[1]
    pair_expert = routes.reshape(-1)
    onehot = (pair_expert[:, None] == jnp.arange(expert_count, dtype=jnp.int32)[None, :]).astype(
        jnp.int32
    )
    earlier = jnp.cumsum(onehot, axis=0) - onehot
    slot_index = jnp.sum(earlier * onehot, axis=1)
    target = pair_expert * slot_count + slot_index
    pair_total = group_tokens * top_count
    slot_table = (
        jnp.full((expert_count * slot_count,), -1, jnp.int32)
        .at[target]
        .set(jnp.arange(pair_total, dtype=jnp.int32))
    )
    slot_table = slot_table.reshape(expert_count, slot_count)
    filled = slot_table >= 0
    token_ids = jnp.maximum(slot_table, 0) // top_count
    row_block = jnp.where(filled[:, :, None], group_input[token_ids], jnp.zeros((), jnp.bfloat16))
    recv_rows = lax.all_to_all(row_block, "expert", split_axis=0, concat_axis=0, tiled=True)
    sources = recv_rows.shape[0]
    quarter = recv_rows.shape[2]
    rows = recv_rows.reshape(sources * slot_count, quarter)
    pre_blocks = jnp.einsum(
        "rd,jdh->jrh", rows, w_blocks[:, 0], preferred_element_type=jnp.float32
    ).astype(jnp.bfloat16)
    pre_terms = lax.all_to_all(pre_blocks, "tensor", split_axis=0, concat_axis=0)
    pre_value = jnp.sum(pre_terms.astype(jnp.float32), axis=0)
    hidden_part = jax.nn.silu(pre_value).astype(jnp.bfloat16)
    hidden_copies = jnp.broadcast_to(hidden_part[None], (tensor_count,) + hidden_part.shape)
    hidden_blocks = lax.all_to_all(hidden_copies, "tensor", split_axis=0, concat_axis=0)
    summed = jnp.zeros((rows.shape[0], quarter), jnp.float32)
    for lane in range(tensor_count):
        term = lax.dot_general(
            hidden_blocks[lane],
            w_blocks[lane, 1],
            (((1,), (1,)), ((), ())),
            preferred_element_type=jnp.float32,
        ).astype(jnp.bfloat16)
        summed = summed + term.astype(jnp.float32)
    expert_out = summed.astype(jnp.bfloat16).reshape(sources, slot_count, quarter)
    returned = lax.all_to_all(expert_out, "expert", split_axis=0, concat_axis=0, tiled=True)
    flat_back = returned.reshape(expert_count * slot_count, quarter)
    picked = flat_back[target].astype(jnp.float32) * gate_weights.reshape(-1)[:, None]
    mixture = jnp.sum(picked.reshape(group_tokens, top_count, quarter), axis=1)
    out_part = (group_resid.astype(jnp.float32) + mixture).astype(jnp.bfloat16)
    out_copies = jnp.broadcast_to(out_part[None], (tensor_count,) + out_part.shape)
    out_blocks = lax.all_to_all(out_copies, "tensor", split_axis=0, concat_axis=0)
    return out_blocks.transpose(1, 0, 2).reshape(group_tokens, model_width)


def solution(mesh):
    return jax.shard_map(
        layer,
        mesh=mesh,
        in_specs=(
            P("tensor", "expert", None),
            P(("expert", "tensor"), None),
            P(),
            P("expert", None, "tensor"),
            P("expert", "tensor", None),
            P("expert", None),
            P("expert", None),
        ),
        out_specs=P("expert", None),
        check_vma=False,
    )
```

```python
import jax
import jax.numpy as jnp
from jax import lax
from jax.sharding import PartitionSpec as P

QB = 128


EPSILON = 1e-06


def capacity(group_tokens, top_count, expert_count):
    return min(group_tokens, max(4, 2 * group_tokens * top_count // expert_count))


def layer(attn_partial, residual_in, norm_gain, w_in, w_out, routes, gate_weights):
    group_tokens, top_count = routes.shape
    model_width = residual_in.shape[1]
    expert_count = lax.axis_size("expert")
    tensor_count = lax.axis_size("tensor")
    slot_count = capacity(group_tokens, top_count, expert_count)
    block_count = model_width // QB
    w_stack = jnp.stack([w_in[0], w_out[0].T])
    width_quarter = model_width // tensor_count
    own = lax.axis_index("tensor")
    pieces = [lax.dynamic_slice_in_dim(w_stack, own * width_quarter, width_quarter, axis=1)]
    for shift in range(1, tensor_count):
        chunk = lax.dynamic_slice_in_dim(
            w_stack, ((own + shift) % tensor_count) * width_quarter, width_quarter, axis=1
        )
        ring = [(u, (u + shift) % tensor_count) for u in range(tensor_count)]
        pieces.append(lax.ppermute(chunk, "tensor", ring))
    by_shift = jnp.stack(pieces)
    w_blocks = by_shift[(own - jnp.arange(tensor_count)) % tensor_count]

    head_terms = lax.all_to_all(
        attn_partial[0].reshape(tensor_count, -1, model_width), "tensor", split_axis=0, concat_axis=0
    )
    attention = jnp.sum(head_terms.astype(jnp.float32), axis=0)
    residual = (residual_in.astype(jnp.float32) + attention).astype(jnp.bfloat16)
    stream = residual.astype(jnp.float32)
    rms_value = jnp.sqrt(jnp.mean(stream * stream, axis=1, keepdims=True) + EPSILON)
    normed = stream / rms_value * norm_gain.astype(jnp.float32)
    blocks = normed.reshape(-1, block_count, QB)
    block_scale = (jnp.max(jnp.abs(blocks), axis=2) + EPSILON).astype(jnp.bfloat16)
    scale_wide = block_scale.astype(jnp.float32)[:, :, None]
    quantized = (blocks / scale_wide).astype(jnp.bfloat16)
    expert_input = (
        (quantized.astype(jnp.float32) * scale_wide).reshape(-1, model_width).astype(jnp.bfloat16)
    )
    token_rows = expert_input.shape[0]
    both_rows = jnp.concatenate([expert_input, residual], axis=0)
    both_rows = both_rows.reshape(2 * token_rows, tensor_count, -1).transpose(1, 0, 2)
    both = lax.all_to_all(both_rows, "tensor", split_axis=0, concat_axis=0)
    group_input = both[:, :token_rows].reshape(group_tokens, -1)
    group_resid = both[:, token_rows:].reshape(group_tokens, -1)
    pair_expert = routes.reshape(-1)
    onehot = (pair_expert[:, None] == jnp.arange(expert_count, dtype=jnp.int32)[None, :]).astype(
        jnp.int32
    )
    earlier = jnp.cumsum(onehot, axis=0) - onehot
    slot_index = jnp.sum(earlier * onehot, axis=1)
    target = pair_expert * slot_count + slot_index
    pair_total = group_tokens * top_count
    slot_table = (
        jnp.full((expert_count * slot_count,), -1, jnp.int32)
        .at[target]
        .set(jnp.arange(pair_total, dtype=jnp.int32))
    )
    slot_table = slot_table.reshape(expert_count, slot_count)
    filled = slot_table >= 0
    token_ids = jnp.maximum(slot_table, 0) // top_count
    row_block = jnp.where(filled[:, :, None], group_input[token_ids], jnp.zeros((), jnp.bfloat16))
    recv_rows = lax.all_to_all(row_block, "expert", split_axis=0, concat_axis=0, tiled=True)
    sources = recv_rows.shape[0]
    quarter = recv_rows.shape[2]
    rows = recv_rows.reshape(sources * slot_count, quarter)
    pre_blocks = jnp.einsum(
        "rd,jdh->jrh", rows, w_blocks[:, 0], preferred_element_type=jnp.float32
    ).astype(jnp.bfloat16)
    pre_terms = lax.all_to_all(pre_blocks, "tensor", split_axis=0, concat_axis=0)
    pre_value = jnp.sum(pre_terms.astype(jnp.float32), axis=0)
    hidden_part = jax.nn.silu(pre_value).astype(jnp.bfloat16)
    hidden_copies = jnp.broadcast_to(hidden_part[None], (tensor_count,) + hidden_part.shape)
    hidden_blocks = lax.all_to_all(hidden_copies, "tensor", split_axis=0, concat_axis=0)
    summed = jnp.zeros((rows.shape[0], quarter), jnp.float32)
    for lane in range(tensor_count):
        term = lax.dot_general(
            hidden_blocks[lane],
            w_blocks[lane, 1],
            (((1,), (1,)), ((), ())),
            preferred_element_type=jnp.float32,
        ).astype(jnp.bfloat16)
        summed = summed + term.astype(jnp.float32)
    expert_out = summed.astype(jnp.bfloat16).reshape(sources, slot_count, quarter)
    returned = lax.all_to_all(expert_out, "expert", split_axis=0, concat_axis=0, tiled=True)
    flat_back = returned.reshape(expert_count * slot_count, quarter)
    picked = flat_back[target].astype(jnp.float32) * gate_weights.reshape(-1)[:, None]
    mixture = jnp.sum(picked.reshape(group_tokens, top_count, quarter), axis=1)
    out_part = (group_resid.astype(jnp.float32) + mixture).astype(jnp.bfloat16)
    out_copies = jnp.broadcast_to(out_part[None], (tensor_count,) + out_part.shape)
    out_blocks = lax.all_to_all(out_copies, "tensor", split_axis=0, concat_axis=0)
    return out_blocks.transpose(1, 0, 2).reshape(group_tokens, model_width)


def solution(mesh):
    return jax.shard_map(
        layer,
        mesh=mesh,
        in_specs=(
            P("tensor", "expert", None),
            P(("expert", "tensor"), None),
            P(),
            P("expert", None, "tensor"),
            P("expert", "tensor", None),
            P("expert", None),
            P("expert", None),
        ),
        out_specs=P("expert", None),
        check_vma=False,
    )
```

```python
import jax
import jax.numpy as jnp
from jax import lax
from jax.sharding import PartitionSpec as P

QB = 128


EPSILON = 1e-06


def capacity(group_tokens, top_count, expert_count):
    return min(group_tokens, max(4, 2 * group_tokens * top_count // expert_count))


def layer(attn_partial, residual_in, norm_gain, w_in, w_out, routes, gate_weights):
    group_tokens, top_count = routes.shape
    model_width = residual_in.shape[1]
    expert_count = lax.axis_size("expert")
    tensor_count = lax.axis_size("tensor")
    slot_count = capacity(group_tokens, top_count, expert_count)
    block_count = model_width // QB
    w_stack = jnp.stack([w_in[0], w_out[0].T])
    width_quarter = model_width // tensor_count
    own = lax.axis_index("tensor")
    pieces = [lax.dynamic_slice_in_dim(w_stack, own * width_quarter, width_quarter, axis=1)]
    for shift in range(1, tensor_count):
        chunk = lax.dynamic_slice_in_dim(
            w_stack, ((own + shift) % tensor_count) * width_quarter, width_quarter, axis=1
        )
        ring = [(u, (u + shift) % tensor_count) for u in range(tensor_count)]
        pieces.append(lax.ppermute(chunk, "tensor", ring))
    by_shift = jnp.stack(pieces)
    w_blocks = by_shift[(own - jnp.arange(tensor_count)) % tensor_count]

    head_terms = lax.all_to_all(
        attn_partial[0].reshape(tensor_count, -1, model_width), "tensor", split_axis=0, concat_axis=0
    )
    attention = jnp.sum(head_terms.astype(jnp.float32), axis=0)
    residual = (residual_in.astype(jnp.float32) + attention).astype(jnp.bfloat16)
    stream = residual.astype(jnp.float32)
    rms_value = jnp.sqrt(jnp.mean(stream * stream, axis=1, keepdims=True) + EPSILON)
    normed = stream / rms_value * norm_gain.astype(jnp.float32)
    blocks = normed.reshape(-1, block_count, QB)
    block_scale = (jnp.max(jnp.abs(blocks), axis=2) + EPSILON).astype(jnp.bfloat16)
    scale_wide = block_scale.astype(jnp.float32)[:, :, None]
    quantized = (blocks / scale_wide).astype(jnp.bfloat16)
    expert_input = (
        (quantized.astype(jnp.float32) * scale_wide).reshape(-1, model_width).astype(jnp.bfloat16)
    )
    token_rows = expert_input.shape[0]
    both_rows = jnp.concatenate([expert_input, residual], axis=0)
    both_rows = both_rows.reshape(2 * token_rows, tensor_count, -1).transpose(1, 0, 2)
    both = lax.all_to_all(both_rows, "tensor", split_axis=0, concat_axis=0)
    group_input = both[:, :token_rows].reshape(group_tokens, -1)
    group_resid = both[:, token_rows:].reshape(group_tokens, -1)
    pair_expert = routes.reshape(-1)
    onehot = (pair_expert[:, None] == jnp.arange(expert_count, dtype=jnp.int32)[None, :]).astype(
        jnp.int32
    )
    earlier = jnp.cumsum(onehot, axis=0) - onehot
    slot_index = jnp.sum(earlier * onehot, axis=1)
    target = pair_expert * slot_count + slot_index
    pair_total = group_tokens * top_count
    slot_table = (
        jnp.full((expert_count * slot_count,), -1, jnp.int32)
        .at[target]
        .set(jnp.arange(pair_total, dtype=jnp.int32))
    )
    slot_table = slot_table.reshape(expert_count, slot_count)
    filled = slot_table >= 0
    token_ids = jnp.maximum(slot_table, 0) // top_count
    row_block = jnp.where(filled[:, :, None], group_input[token_ids], jnp.zeros((), jnp.bfloat16))
    recv_rows = lax.all_to_all(row_block, "expert", split_axis=0, concat_axis=0, tiled=True)
    sources = recv_rows.shape[0]
    quarter = recv_rows.shape[2]
    rows = recv_rows.reshape(sources * slot_count, quarter)
    pre_blocks = jnp.einsum(
        "rd,jdh->jrh", rows, w_blocks[:, 0], preferred_element_type=jnp.float32
    ).astype(jnp.bfloat16)
    pre_terms = lax.all_to_all(pre_blocks, "tensor", split_axis=0, concat_axis=0)
    pre_value = jnp.sum(pre_terms.astype(jnp.float32), axis=0)
    hidden_part = jax.nn.silu(pre_value).astype(jnp.bfloat16)
    hidden_copies = jnp.broadcast_to(hidden_part[None], (tensor_count,) + hidden_part.shape)
    hidden_blocks = lax.all_to_all(hidden_copies, "tensor", split_axis=0, concat_axis=0)
    terms = jnp.einsum(
        "jrh,jdh->jrd", hidden_blocks, w_blocks[:, 1], preferred_element_type=jnp.float32
    ).astype(jnp.bfloat16)
    summed = jnp.sum(terms.astype(jnp.float32), axis=0)
    expert_out = summed.astype(jnp.bfloat16).reshape(sources, slot_count, quarter)
    returned = lax.all_to_all(expert_out, "expert", split_axis=0, concat_axis=0, tiled=True)
    flat_back = returned.reshape(expert_count * slot_count, quarter)
    picked = flat_back[target].astype(jnp.float32) * gate_weights.reshape(-1)[:, None]
    mixture = jnp.sum(picked.reshape(group_tokens, top_count, quarter), axis=1)
    out_part = (group_resid.astype(jnp.float32) + mixture).astype(jnp.bfloat16)
    out_copies = jnp.broadcast_to(out_part[None], (tensor_count,) + out_part.shape)
    out_blocks = lax.all_to_all(out_copies, "tensor", split_axis=0, concat_axis=0)
    return out_blocks.transpose(1, 0, 2).reshape(group_tokens, model_width)


def solution(mesh):
    return jax.shard_map(
        layer,
        mesh=mesh,
        in_specs=(
            P("tensor", "expert", None),
            P(("expert", "tensor"), None),
            P(),
            P("expert", None, "tensor"),
            P("expert", "tensor", None),
            P("expert", None),
            P("expert", None),
        ),
        out_specs=P("expert", None),
        check_vma=False,
    )
```

```python
import jax
import jax.numpy as jnp
from jax import lax
from jax.sharding import PartitionSpec as P

QB = 128


EPSILON = 1e-06


def capacity(group_tokens, top_count, expert_count):
    return min(group_tokens, max(4, 2 * group_tokens * top_count // expert_count))


def layer(attn_partial, residual_in, norm_gain, w_in, w_out, routes, gate_weights):
    group_tokens, top_count = routes.shape
    model_width = residual_in.shape[1]
    expert_count = lax.axis_size("expert")
    tensor_count = lax.axis_size("tensor")
    slot_count = capacity(group_tokens, top_count, expert_count)
    block_count = model_width // QB
    width_quarter = model_width // tensor_count
    own = lax.axis_index("tensor")

    def swap(weights, axis):
        pieces = [lax.dynamic_slice_in_dim(weights, own * width_quarter, width_quarter, axis=axis)]
        for shift in range(1, tensor_count):
            start = ((own + shift) % tensor_count) * width_quarter
            chunk = lax.dynamic_slice_in_dim(weights, start, width_quarter, axis=axis)
            ring = [(u, (u + shift) % tensor_count) for u in range(tensor_count)]
            pieces.append(lax.ppermute(chunk, "tensor", ring))
        by_shift = jnp.stack(pieces)
        return by_shift[(own - jnp.arange(tensor_count)) % tensor_count]

    w_in_blocks = swap(w_in[0], 0)
    w_out_blocks = swap(w_out[0], 1)

    head_blocks = attn_partial[0].reshape(tensor_count, -1, model_width)
    head_terms = lax.all_to_all(head_blocks, "tensor", split_axis=0, concat_axis=0)
    attention = jnp.sum(head_terms.astype(jnp.float32), axis=0)
    residual = (residual_in.astype(jnp.float32) + attention).astype(jnp.bfloat16)
    stream = residual.astype(jnp.float32)
    rms_value = jnp.sqrt(jnp.mean(stream * stream, axis=1, keepdims=True) + EPSILON)
    normed = stream / rms_value * norm_gain.astype(jnp.float32)
    blocks = normed.reshape(-1, block_count, QB)
    block_scale = (jnp.max(jnp.abs(blocks), axis=2) + EPSILON).astype(jnp.bfloat16)
    scale_wide = block_scale.astype(jnp.float32)[:, :, None]
    quantized = (blocks / scale_wide).astype(jnp.bfloat16)
    expert_input = (
        (quantized.astype(jnp.float32) * scale_wide).reshape(-1, model_width).astype(jnp.bfloat16)
    )
    token_rows = expert_input.shape[0]
    both_rows = jnp.concatenate([expert_input, residual], axis=0)
    both_rows = both_rows.reshape(2 * token_rows, tensor_count, -1).transpose(1, 0, 2)
    both = lax.all_to_all(both_rows, "tensor", split_axis=0, concat_axis=0)
    group_input = both[:, :token_rows].reshape(group_tokens, -1)
    group_resid = both[:, token_rows:].reshape(group_tokens, -1)
    pair_expert = routes.reshape(-1)
    onehot = (pair_expert[:, None] == jnp.arange(expert_count, dtype=jnp.int32)[None, :]).astype(
        jnp.int32
    )
    earlier = jnp.cumsum(onehot, axis=0) - onehot
    slot_index = jnp.sum(earlier * onehot, axis=1)
    target = pair_expert * slot_count + slot_index
    pair_total = group_tokens * top_count
    slot_table = (
        jnp.full((expert_count * slot_count,), -1, jnp.int32)
        .at[target]
        .set(jnp.arange(pair_total, dtype=jnp.int32))
    )
    slot_table = slot_table.reshape(expert_count, slot_count)
    token_ids = jnp.maximum(slot_table, 0) // top_count
    row_block = group_input[token_ids]
    recv_rows = lax.all_to_all(row_block, "expert", split_axis=0, concat_axis=0, tiled=True)
    sources = recv_rows.shape[0]
    quarter = recv_rows.shape[2]
    rows = recv_rows.reshape(sources * slot_count, quarter)
    pre_blocks = jnp.einsum(
        "rd,jdh->jrh", rows, w_in_blocks, preferred_element_type=jnp.float32
    ).astype(jnp.bfloat16)
    pre_terms = lax.all_to_all(pre_blocks, "tensor", split_axis=0, concat_axis=0)
    pre_value = jnp.sum(pre_terms.astype(jnp.float32), axis=0)
    hidden_part = jax.nn.silu(pre_value).astype(jnp.bfloat16)
    hidden_copies = jnp.broadcast_to(hidden_part[None], (tensor_count,) + hidden_part.shape)
    hidden_blocks = lax.all_to_all(hidden_copies, "tensor", split_axis=0, concat_axis=0)
    terms = jnp.einsum(
        "jrh,jhd->jrd", hidden_blocks, w_out_blocks, preferred_element_type=jnp.float32
    ).astype(jnp.bfloat16)
    summed = jnp.sum(terms.astype(jnp.float32), axis=0)
    expert_out = summed.astype(jnp.bfloat16).reshape(sources, slot_count, quarter)
    returned = lax.all_to_all(expert_out, "expert", split_axis=0, concat_axis=0, tiled=True)
    flat_back = returned.reshape(expert_count * slot_count, quarter)
    picked = flat_back[target].astype(jnp.float32) * gate_weights.reshape(-1)[:, None]
    mixture = jnp.sum(picked.reshape(group_tokens, top_count, quarter), axis=1)
    out_part = (group_resid.astype(jnp.float32) + mixture).astype(jnp.bfloat16)
    out_copies = jnp.broadcast_to(out_part[None], (tensor_count,) + out_part.shape)
    out_blocks = lax.all_to_all(out_copies, "tensor", split_axis=0, concat_axis=0)
    return out_blocks.transpose(1, 0, 2).reshape(group_tokens, model_width)


def solution(mesh):
    return jax.shard_map(
        layer,
        mesh=mesh,
        in_specs=(
            P("tensor", "expert", None),
            P(("expert", "tensor"), None),
            P(),
            P("expert", None, "tensor"),
            P("expert", "tensor", None),
            P("expert", None),
            P("expert", None),
        ),
        out_specs=P("expert", None),
        check_vma=False,
    )
```

```python
import jax
import jax.numpy as jnp
from jax import lax
from jax.sharding import PartitionSpec as P

QB = 128


EPSILON = 1e-06


def capacity(group_tokens, top_count, expert_count):
    return min(group_tokens, max(4, 2 * group_tokens * top_count // expert_count))


def layer(attn_partial, residual_in, norm_gain, w_in, w_out, routes, gate_weights):
    group_tokens, top_count = routes.shape
    model_width = residual_in.shape[1]
    expert_count = lax.axis_size("expert")
    tensor_count = lax.axis_size("tensor")
    slot_count = capacity(group_tokens, top_count, expert_count)
    block_count = model_width // QB
    width_quarter = model_width // tensor_count
    own = lax.axis_index("tensor")

    w_stack = jnp.stack([w_in[0], w_out[0].T])
    pieces = [lax.dynamic_slice_in_dim(w_stack, own * width_quarter, width_quarter, axis=1)]
    for shift in range(1, tensor_count):
        start = ((own + shift) % tensor_count) * width_quarter
        chunk = lax.dynamic_slice_in_dim(w_stack, start, width_quarter, axis=1)
        ring = [(u, (u + shift) % tensor_count) for u in range(tensor_count)]
        pieces.append(lax.ppermute(chunk, "tensor", ring))
    by_shift = jnp.stack(pieces)
    w_blocks = by_shift[(own - jnp.arange(tensor_count)) % tensor_count]

    head_terms = lax.all_to_all(
        attn_partial[0].reshape(tensor_count, -1, model_width), "tensor", split_axis=0, concat_axis=0
    )
    attention = jnp.sum(head_terms.astype(jnp.float32), axis=0)
    residual = (residual_in.astype(jnp.float32) + attention).astype(jnp.bfloat16)
    stream = residual.astype(jnp.float32)
    rms_value = jnp.sqrt(jnp.mean(stream * stream, axis=1, keepdims=True) + EPSILON)
    normed = stream / rms_value * norm_gain.astype(jnp.float32)
    blocks = normed.reshape(-1, block_count, QB)
    block_scale = (jnp.max(jnp.abs(blocks), axis=2) + EPSILON).astype(jnp.bfloat16)
    scale_wide = block_scale.astype(jnp.float32)[:, :, None]
    quantized = (blocks / scale_wide).astype(jnp.bfloat16)
    expert_input = (
        (quantized.astype(jnp.float32) * scale_wide).reshape(-1, model_width).astype(jnp.bfloat16)
    )
    token_rows = expert_input.shape[0]
    both_rows = jnp.concatenate([expert_input, residual], axis=0)
    both_rows = both_rows.reshape(2 * token_rows, tensor_count, -1).transpose(1, 0, 2)
    both = lax.all_to_all(both_rows, "tensor", split_axis=0, concat_axis=0)
    group_input = both[:, :token_rows].reshape(group_tokens, -1)
    group_resid = both[:, token_rows:].reshape(group_tokens, -1)
    pair_expert = routes.reshape(-1)
    onehot = (pair_expert[:, None] == jnp.arange(expert_count, dtype=jnp.int32)[None, :]).astype(
        jnp.int32
    )
    earlier = jnp.cumsum(onehot, axis=0) - onehot
    slot_index = jnp.sum(earlier * onehot, axis=1)
    target = pair_expert * slot_count + slot_index
    pair_total = group_tokens * top_count
    slot_table = (
        jnp.full((expert_count * slot_count,), -1, jnp.int32)
        .at[target]
        .set(jnp.arange(pair_total, dtype=jnp.int32))
    )
    slot_table = slot_table.reshape(expert_count, slot_count)
    filled = slot_table >= 0
    token_ids = jnp.maximum(slot_table, 0) // top_count
    row_block = jnp.where(filled[:, :, None], group_input[token_ids], jnp.zeros((), jnp.bfloat16))
    recv_rows = lax.all_to_all(row_block, "expert", split_axis=0, concat_axis=0, tiled=True)
    sources = recv_rows.shape[0]
    quarter = recv_rows.shape[2]
    rows = recv_rows.reshape(sources * slot_count, quarter)
    pre_blocks = jnp.einsum(
        "rd,jdh->jrh", rows, w_blocks[:, 0], preferred_element_type=jnp.float32
    ).astype(jnp.bfloat16)
    pre_terms = lax.all_to_all(pre_blocks, "tensor", split_axis=0, concat_axis=0)
    pre_value = jnp.sum(pre_terms.astype(jnp.float32), axis=0)
    hidden_part = jax.nn.silu(pre_value).astype(jnp.bfloat16)
    hidden_copies = jnp.broadcast_to(hidden_part[None], (tensor_count,) + hidden_part.shape)
    hidden_blocks = lax.all_to_all(hidden_copies, "tensor", split_axis=0, concat_axis=0)
    terms = jnp.einsum(
        "jrh,jdh->jrd", hidden_blocks, w_blocks[:, 1], preferred_element_type=jnp.float32
    ).astype(jnp.bfloat16)
    summed = jnp.sum(terms.astype(jnp.float32), axis=0)
    expert_out = summed.astype(jnp.bfloat16).reshape(sources, slot_count, quarter)
    returned = lax.all_to_all(expert_out, "expert", split_axis=0, concat_axis=0, tiled=True)
    flat_back = returned.reshape(expert_count * slot_count, quarter)
    picked = flat_back[target].astype(jnp.float32) * gate_weights.reshape(-1)[:, None]
    mixture = jnp.sum(picked.reshape(group_tokens, top_count, quarter), axis=1)
    out_part = (group_resid.astype(jnp.float32) + mixture).astype(jnp.bfloat16)
    out_copies = jnp.broadcast_to(out_part[None], (tensor_count,) + out_part.shape)
    out_blocks = lax.all_to_all(out_copies, "tensor", split_axis=0, concat_axis=0)
    return out_blocks.transpose(1, 0, 2).reshape(group_tokens, model_width)


def solution(mesh):
    return jax.shard_map(
        layer,
        mesh=mesh,
        in_specs=(
            P("tensor", "expert", None),
            P(("expert", "tensor"), None),
            P(),
            P("expert", None, "tensor"),
            P("expert", "tensor", None),
            P("expert", None),
            P("expert", None),
        ),
        out_specs=P("expert", None),
        check_vma=False,
    )
```

```python
import jax
import jax.numpy as jnp
from jax import lax
from jax.sharding import PartitionSpec as P

QB = 128


EPSILON = 1e-06


def capacity(group_tokens, top_count, expert_count):
    return min(group_tokens, max(4, 2 * group_tokens * top_count // expert_count))


def layer(attn_partial, residual_in, norm_gain, w_in, w_out, routes, gate_weights):
    group_tokens, top_count = routes.shape
    model_width = residual_in.shape[1]
    expert_count = lax.axis_size("expert")
    tensor_count = lax.axis_size("tensor")
    slot_count = capacity(group_tokens, top_count, expert_count)
    block_count = model_width // QB
    width_quarter = model_width // tensor_count
    own = lax.axis_index("tensor")

    def swap(weights, axis):
        pieces = [lax.dynamic_slice_in_dim(weights, own * width_quarter, width_quarter, axis=axis)]
        for shift in range(1, tensor_count):
            start = ((own + shift) % tensor_count) * width_quarter
            chunk = lax.dynamic_slice_in_dim(weights, start, width_quarter, axis=axis)
            ring = [(u, (u + shift) % tensor_count) for u in range(tensor_count)]
            pieces.append(lax.ppermute(chunk, "tensor", ring))
        by_shift = jnp.stack(pieces)
        return by_shift[(own - jnp.arange(tensor_count)) % tensor_count]

    w_in_blocks = swap(w_in[0], 0)
    w_out_blocks = swap(w_out[0], 1)

    head_terms = lax.all_to_all(
        attn_partial[0].reshape(tensor_count, -1, model_width), "tensor", split_axis=0, concat_axis=0
    )
    attention = jnp.sum(head_terms.astype(jnp.float32), axis=0)
    residual = (residual_in.astype(jnp.float32) + attention).astype(jnp.bfloat16)
    stream = residual.astype(jnp.float32)
    rms_value = jnp.sqrt(jnp.mean(stream * stream, axis=1, keepdims=True) + EPSILON)
    normed = stream / rms_value * norm_gain.astype(jnp.float32)
    blocks = normed.reshape(-1, block_count, QB)
    block_scale = (jnp.max(jnp.abs(blocks), axis=2) + EPSILON).astype(jnp.bfloat16)
    scale_wide = block_scale.astype(jnp.float32)[:, :, None]
    quantized = (blocks / scale_wide).astype(jnp.bfloat16)
    expert_input = (
        (quantized.astype(jnp.float32) * scale_wide).reshape(-1, model_width).astype(jnp.bfloat16)
    )
    token_rows = expert_input.shape[0]
    both_rows = jnp.concatenate([expert_input, residual], axis=0)
    both_rows = both_rows.reshape(2 * token_rows, tensor_count, -1).transpose(1, 0, 2)
    both = lax.all_to_all(both_rows, "tensor", split_axis=0, concat_axis=0)
    group_input = both[:, :token_rows].reshape(group_tokens, -1)
    group_resid = both[:, token_rows:].reshape(group_tokens, -1)
    pair_expert = routes.reshape(-1)
    onehot = (pair_expert[:, None] == jnp.arange(expert_count, dtype=jnp.int32)[None, :]).astype(
        jnp.int32
    )
    earlier = jnp.cumsum(onehot, axis=0) - onehot
    slot_index = jnp.sum(earlier * onehot, axis=1)
    target = pair_expert * slot_count + slot_index
    pair_total = group_tokens * top_count
    slot_table = (
        jnp.full((expert_count * slot_count,), -1, jnp.int32)
        .at[target]
        .set(jnp.arange(pair_total, dtype=jnp.int32))
    )
    slot_table = slot_table.reshape(expert_count, slot_count)
    token_ids = jnp.maximum(slot_table, 0) // top_count
    pick = (token_ids[:, :, None] == jnp.arange(group_tokens)[None, None, :]).astype(jnp.bfloat16)
    row_block = jnp.einsum("esk,kd->esd", pick, group_input, preferred_element_type=jnp.bfloat16)
    recv_rows = lax.all_to_all(row_block, "expert", split_axis=0, concat_axis=0, tiled=True)
    sources = recv_rows.shape[0]
    quarter = recv_rows.shape[2]
    rows = recv_rows.reshape(sources * slot_count, quarter)
    pre_blocks = jnp.einsum(
        "rd,jdh->jrh", rows, w_in_blocks, preferred_element_type=jnp.float32
    ).astype(jnp.bfloat16)
    pre_terms = lax.all_to_all(pre_blocks, "tensor", split_axis=0, concat_axis=0)
    pre_value = jnp.sum(pre_terms.astype(jnp.float32), axis=0)
    hidden_part = jax.nn.silu(pre_value).astype(jnp.bfloat16)
    hidden_copies = jnp.broadcast_to(hidden_part[None], (tensor_count,) + hidden_part.shape)
    hidden_blocks = lax.all_to_all(hidden_copies, "tensor", split_axis=0, concat_axis=0)
    terms = jnp.einsum(
        "jrh,jhd->jrd", hidden_blocks, w_out_blocks, preferred_element_type=jnp.float32
    ).astype(jnp.bfloat16)
    summed = jnp.sum(terms.astype(jnp.float32), axis=0)
    expert_out = summed.astype(jnp.bfloat16).reshape(sources, slot_count, quarter)
    returned = lax.all_to_all(expert_out, "expert", split_axis=0, concat_axis=0, tiled=True)
    flat_back = returned.reshape(expert_count * slot_count, quarter)
    picked = flat_back[target].astype(jnp.float32) * gate_weights.reshape(-1)[:, None]
    mixture = jnp.sum(picked.reshape(group_tokens, top_count, quarter), axis=1)
    out_part = (group_resid.astype(jnp.float32) + mixture).astype(jnp.bfloat16)
    out_copies = jnp.broadcast_to(out_part[None], (tensor_count,) + out_part.shape)
    out_blocks = lax.all_to_all(out_copies, "tensor", split_axis=0, concat_axis=0)
    return out_blocks.transpose(1, 0, 2).reshape(group_tokens, model_width)


def solution(mesh):
    return jax.shard_map(
        layer,
        mesh=mesh,
        in_specs=(
            P("tensor", "expert", None),
            P(("expert", "tensor"), None),
            P(),
            P("expert", None, "tensor"),
            P("expert", "tensor", None),
            P("expert", None),
            P("expert", None),
        ),
        out_specs=P("expert", None),
        check_vma=False,
    )
```
